128 devices in a mesh: expert: 16 (over z, x), dp: 8 (over y, core).
Axes of the slice: x: 4, y: 4, z: 4, core: 2. Of those that a mesh axis runs over, the one named last changes fastest.
Arguments:
- tokens: bfloat16 [16, 480, 7168], P('expert', 'dp'), may hold values from -6 to 6
- cotangent: bfloat16 [16, 480, 7168], P('expert', 'dp'), may hold values from -1.5 to 1.5
- counts: int32 [16, 8], replicated, may hold values from 1 to 60, as said below
- w_gate: bfloat16 [16, 7168, 2048], P('expert', None, 'dp'), may hold values from -0.0625 to 0.0625
- w_up: bfloat16 [16, 7168, 2048], P('expert', None, 'dp'), may hold values from -0.0625 to 0.0625
- w_down: bfloat16 [16, 2048, 7168], P('expert', 'dp'), may hold values from -0.125 to 0.125
Outputs:
- outputs: bfloat16 [16, 480, 7168], P('expert', 'dp')
- input_grads: bfloat16 [16, 480, 7168], P('expert', 'dp')
- gate_grad: bfloat16 [16, 7168, 2048], P('expert', None, 'dp')
- up_grad: bfloat16 [16, 7168, 2048], P('expert', None, 'dp')
- down_grad: bfloat16 [16, 2048, 7168], P('expert', 'dp')
The draws below stay inside these ranges and needn't reach their ends.
Inputs may be any that keep to these rules, and one draw needn't show every extreme that they name: For each expert e below 8, exactly one of experts e and e + 8 is hot: all its counts exceed 40 - 20 and one equals 60; every count of the other is at most 20 and one equals 20.
All inputs are finite; a program needn't handle non-finite values.
Results may differ from the reference program's by a relative error of at most 0.012.
Values may be sent and summed in bfloat16 or wider, within the bound.
No kernel may reach another device: no remote copies, remote signals or barrier semaphores. Data moves between devices by JAX's collectives and lax.ppermute only.
A program may use at most 192 MiB of HBM per device.

```python
import jax
import jax.numpy as jnp
from jax import lax

D = 7168
H = 2048
HOME = 40
SPILL = 20
CAP = 60
EXPERTS = 16
BATCHES = 8


def draw_counts(key, part):
    keys = jax.random.split(key, 5)
    half = EXPERTS // 2
    border = HOME - SPILL
    side = jax.random.randint(keys[0], (half, 1), 0, 2)
    hot_vals = jax.random.randint(keys[1], (half, BATCHES), border + 1, CAP + 1)
    cold_vals = jax.random.randint(keys[2], (half, BATCHES), 1, border + 1)
    batch_ids = jnp.arange(BATCHES)[None, :]
    hot_full = jax.random.randint(keys[3], (half, 1), 0, BATCHES)
    cold_full = jax.random.randint(keys[4], (half, 1), 0, BATCHES)
    hot_vals = jnp.where(batch_ids == hot_full, CAP, hot_vals)
    cold_vals = jnp.where(batch_ids == cold_full, border, cold_vals)
    lower = jnp.where(side == 0, hot_vals, cold_vals)
    upper = jnp.where(side == 0, cold_vals, hot_vals)
    return jnp.concatenate([lower, upper], axis=0).astype(jnp.int32)


def shard_levels(key, shape, cuts, low, high):
    def one(axis_at, blocks):
        draws = jax.random.uniform(jax.random.fold_in(jax.random.fold_in(key, 6), axis_at), (blocks,), jnp.float32, low / len(cuts), high / len(cuts))
        return jnp.repeat(jnp.exp(draws), shape[axis_at] // blocks).reshape((-1,) + (1,) * (len(shape) - axis_at - 1))

    factor_of = one(*cuts[0])
    for cut in cuts[1:]:
        factor_of = factor_of * one(*cut)
    return factor_of


def normal_values(key, extent, scale, reach, pieces=(), held_as=jnp.bfloat16):
    array = scale * jax.random.normal(key, extent, jnp.float32)
    if pieces:
        array = array * shard_levels(key, extent, pieces, -0.22, 0.18)
    return jnp.clip(array, -reach, reach).astype(held_as)


def setup_inputs(seed: int = 0) -> dict:
    splits = jax.random.split(jax.random.key(seed), 7)
    tokens = normal_values(splits[0], (EXPERTS, BATCHES * CAP, D), 1.0, 6.0, ((0, 16), (1, 8)))
    cotangent = normal_values(splits[1], (EXPERTS, BATCHES * CAP, D), 0.25, 1.5, ((0, 16), (1, 8)))
    counts = draw_counts(jax.random.fold_in(splits[6], 71), 0)
    w_gate = normal_values(splits[3], (EXPERTS, D, H), D ** -0.5, 0.0625, ((0, 16), (2, 8)))
    w_up = normal_values(splits[4], (EXPERTS, D, H), D ** -0.5, 0.0625, ((0, 16), (2, 8)))
    w_down = normal_values(splits[5], (EXPERTS, H, D), H ** -0.5, 0.125, ((0, 16), (1, 8)))
    return {"tokens": tokens, "cotangent": cotangent, "counts": counts, "w_gate": w_gate, "w_up": w_up, "w_down": w_down}


def silu_slope(value):
    sigma = jax.nn.sigmoid(value)
    return sigma * (1.0 + value * (1.0 - sigma))


def slice_total(parts):
    rounded = lax.optimization_barrier(parts.astype(jnp.bfloat16))
    return jnp.sum(rounded.astype(jnp.float32), axis=0).astype(jnp.bfloat16)


def one_expert(operands):
    rows_in, cot_in, count_row, gate_w, up_w, down_w = operands
    width = H // BATCHES
    valid = (jnp.arange(CAP, dtype=jnp.int32)[None, :] < count_row[:, None])[:, :, None]
    masked = jnp.where(valid, rows_in, jnp.zeros_like(rows_in))
    masked_cot = jnp.where(valid, cot_in, jnp.zeros_like(cot_in))
    flat = masked.reshape(BATCHES * CAP, D)
    flat_cot = masked_cot.reshape(BATCHES * CAP, D)
    gate = jnp.dot(flat, gate_w, preferred_element_type=jnp.float32)
    up = jnp.dot(flat, up_w, preferred_element_type=jnp.float32)
    active = jax.nn.silu(gate)
    hidden = (active * up).astype(jnp.bfloat16)
    out_parts = jnp.einsum("rbh,bhd->brd", hidden.reshape(-1, BATCHES, width).astype(jnp.float32),
                           down_w.reshape(BATCHES, width, D).astype(jnp.float32), precision=lax.Precision.HIGHEST)
    outputs = slice_total(out_parts)
    hidden_grad = jnp.dot(flat_cot, down_w.T, preferred_element_type=jnp.float32)
    gate_act = (hidden_grad * up * silu_slope(gate)).astype(jnp.bfloat16)
    up_act = (hidden_grad * active).astype(jnp.bfloat16)
    in_parts = jnp.einsum("rbh,dbh->brd", gate_act.reshape(-1, BATCHES, width).astype(jnp.float32),
                          gate_w.reshape(D, BATCHES, width).astype(jnp.float32), precision=lax.Precision.HIGHEST)
    in_parts = in_parts + jnp.einsum("rbh,dbh->brd", up_act.reshape(-1, BATCHES, width).astype(jnp.float32),
                                     up_w.reshape(D, BATCHES, width).astype(jnp.float32), precision=lax.Precision.HIGHEST)
    input_grads = slice_total(in_parts)

    def split_rows(values):
        shaped = values.reshape(BATCHES, CAP, values.shape[-1])
        return shaped[:, :HOME].reshape(-1, values.shape[-1]), shaped[:, HOME:].reshape(-1, values.shape[-1])

    rows_home, rows_spill = split_rows(flat)
    cot_home, cot_spill = split_rows(flat_cot)
    hid_home, hid_spill = split_rows(hidden)
    ga_home, ga_spill = split_rows(gate_act)
    ua_home, ua_spill = split_rows(up_act)

    def combine(home_term, spill_term):
        spill_round = lax.optimization_barrier(spill_term.astype(jnp.bfloat16))
        return (home_term + spill_round.astype(jnp.float32)).astype(jnp.bfloat16)

    gate_grad = combine(jnp.dot(rows_home.T, ga_home, preferred_element_type=jnp.float32),
                        jnp.dot(rows_spill.T, ga_spill, preferred_element_type=jnp.float32))
    up_grad = combine(jnp.dot(rows_home.T, ua_home, preferred_element_type=jnp.float32),
                      jnp.dot(rows_spill.T, ua_spill, preferred_element_type=jnp.float32))
    down_grad = combine(jnp.dot(hid_home.T, cot_home, preferred_element_type=jnp.float32),
                        jnp.dot(hid_spill.T, cot_spill, preferred_element_type=jnp.float32))
    return outputs, input_grads, gate_grad, up_grad, down_grad


def reference(tokens, cotangent, counts, w_gate, w_up, w_down):
    rows_all = tokens.reshape(EXPERTS, BATCHES, CAP, D)
    cot_all = cotangent.reshape(EXPERTS, BATCHES, CAP, D)
    outputs, input_grads, gate_grad, up_grad, down_grad = lax.map(
        one_expert, (rows_all, cot_all, counts, w_gate, w_up, w_down))
    return (outputs.reshape(EXPERTS, BATCHES * CAP, D), input_grads.reshape(EXPERTS, BATCHES * CAP, D),
            gate_grad, up_grad, down_grad)
```

```python
import jax
import jax.numpy as jnp
from jax import lax
from jax.sharding import PartitionSpec as P


def silu_slope(value):
    sigma = jax.nn.sigmoid(value)
    return sigma * (1.0 + value * (1.0 - sigma))


def contract_last(left, right):
    return lax.dot_general(
        left, right, (((1,), (1,)), ((), ())), preferred_element_type=jnp.float32
    )


def contract_first(left, right):
    return lax.dot_general(
        left, right, (((0,), (0,)), ((), ())), preferred_element_type=jnp.float32
    )


def expert_work(rows, cot_rows, gate_w, up_w, down_w):
    gate = jnp.dot(rows, gate_w, preferred_element_type=jnp.float32)
    up = jnp.dot(rows, up_w, preferred_element_type=jnp.float32)
    active = jax.nn.silu(gate)
    hidden = (active * up).astype(jnp.bfloat16)
    out_part = jnp.dot(hidden, down_w, preferred_element_type=jnp.float32)
    hidden_grad = contract_last(cot_rows, down_w)
    gate_act = (hidden_grad * up * silu_slope(gate)).astype(jnp.bfloat16)
    up_act = (hidden_grad * active).astype(jnp.bfloat16)
    in_part = contract_last(gate_act, gate_w) + contract_last(up_act, up_w)
    gate_term = contract_first(rows, gate_act)
    up_term = contract_first(rows, up_act)
    down_term = contract_first(hidden, cot_rows)
    return (out_part, in_part, gate_term, up_term, down_term)


def shards(tokens, cotangent, counts, w_gate, w_up, w_down):
    rows_in = tokens[0]
    cot_in = cotangent[0]
    gate_w = w_gate[0]
    up_w = w_up[0]
    down_w = w_down[0]
    expert_pos = lax.axis_index("expert")
    batch_pos = lax.axis_index("dp")
    expert_ids = jnp.arange(counts.shape[0], dtype=jnp.int32)
    batch_ids = jnp.arange(counts.shape[1], dtype=jnp.int32)
    own_counts = jnp.sum(jnp.where(expert_ids[:, None] == expert_pos, counts, 0), axis=0)
    own_total = jnp.sum(jnp.where(batch_ids == batch_pos, own_counts, 0))
    slots = rows_in.shape[0]
    valid = (jnp.arange(slots, dtype=jnp.int32) < own_total)[:, None]
    masked = jnp.where(valid, rows_in, jnp.zeros_like(rows_in))
    masked_cot = jnp.where(valid, cot_in, jnp.zeros_like(cot_in))
    all_rows = lax.all_gather(masked, "dp", axis=0, tiled=True)
    all_cot = lax.all_gather(masked_cot, "dp", axis=0, tiled=True)
    out_part, in_part, gate_term, up_term, down_term = expert_work(
        all_rows, all_cot, gate_w, up_w, down_w
    )
    outputs = lax.psum_scatter(
        out_part.astype(jnp.bfloat16), "dp", scatter_dimension=0, tiled=True
    )
    input_grads = lax.psum_scatter(
        in_part.astype(jnp.bfloat16), "dp", scatter_dimension=0, tiled=True
    )
    gate_grad = gate_term.astype(jnp.bfloat16)
    up_grad = up_term.astype(jnp.bfloat16)
    down_grad = down_term.astype(jnp.bfloat16)
    return (outputs[None], input_grads[None], gate_grad[None], up_grad[None], down_grad[None])


def solution(mesh):
    placed = (
        P("expert", "dp", None),
        P("expert", "dp", None),
        P(),
        P("expert", None, "dp"),
        P("expert", None, "dp"),
        P("expert", "dp", None),
    )
    return jax.shard_map(
        shards,
        mesh=mesh,
        in_specs=placed,
        out_specs=(
            P("expert", "dp", None),
            P("expert", "dp", None),
            P("expert", None, "dp"),
            P("expert", None, "dp"),
            P("expert", "dp", None),
        ),
        check_vma=False,
    )
```

```python
import jax
import jax.numpy as jnp
from jax import lax
from jax.sharding import PartitionSpec as P


def silu_slope(value):
    sigma = jax.nn.sigmoid(value)
    return sigma * (1.0 + value * (1.0 - sigma))


def contract_last(left, right):
    return lax.dot_general(
        left, right, (((1,), (1,)), ((), ())), preferred_element_type=jnp.float32
    )


def contract_first(left, right):
    return lax.dot_general(
        left, right, (((0,), (0,)), ((), ())), preferred_element_type=jnp.float32
    )


def expert_work(rows, cot_rows, gate_w, up_w, down_w):
    gate = jnp.dot(rows, gate_w, preferred_element_type=jnp.float32)
    up = jnp.dot(rows, up_w, preferred_element_type=jnp.float32)
    active = jax.nn.silu(gate)
    hidden = (active * up).astype(jnp.bfloat16)
    out_part = jnp.dot(hidden, down_w, preferred_element_type=jnp.float32)
    hidden_grad = contract_last(cot_rows, down_w)
    gate_act = (hidden_grad * up * silu_slope(gate)).astype(jnp.bfloat16)
    up_act = (hidden_grad * active).astype(jnp.bfloat16)
    in_part = contract_last(gate_act, gate_w) + contract_last(up_act, up_w)
    gate_term = contract_first(rows, gate_act)
    up_term = contract_first(rows, up_act)
    down_term = contract_first(hidden, cot_rows)
    return (out_part, in_part, gate_term, up_term, down_term)


def shards(tokens, cotangent, counts, w_gate, w_up, w_down):
    rows_in = tokens[0]
    cot_in = cotangent[0]
    gate_w = w_gate[0]
    up_w = w_up[0]
    down_w = w_down[0]
    expert_pos = lax.axis_index("expert")
    batch_pos = lax.axis_index("dp")
    expert_ids = jnp.arange(counts.shape[0], dtype=jnp.int32)
    batch_ids = jnp.arange(counts.shape[1], dtype=jnp.int32)
    own_counts = jnp.sum(jnp.where(expert_ids[:, None] == expert_pos, counts, 0), axis=0)
    own_total = jnp.sum(jnp.where(batch_ids == batch_pos, own_counts, 0))
    slots = rows_in.shape[0]
    valid = (jnp.arange(slots, dtype=jnp.int32) < own_total)[:, None]
    masked = jnp.where(valid, rows_in, jnp.zeros_like(rows_in))
    masked_cot = jnp.where(valid, cot_in, jnp.zeros_like(cot_in))
    all_rows = lax.all_gather(masked, "dp", axis=0, tiled=True)
    all_cot = lax.all_gather(masked_cot, "dp", axis=0, tiled=True)
    out_part, in_part, gate_term, up_term, down_term = expert_work(
        all_rows, all_cot, gate_w, up_w, down_w
    )
    groups = lax.axis_size("dp")
    outputs = lax.psum_scatter(
        out_part.astype(jnp.bfloat16).reshape(groups, slots, -1), "dp", scatter_dimension=0, tiled=False
    )
    input_grads = lax.psum_scatter(
        in_part.astype(jnp.bfloat16).reshape(groups, slots, -1), "dp", scatter_dimension=0, tiled=False
    )
    gate_grad = gate_term.astype(jnp.bfloat16)
    up_grad = up_term.astype(jnp.bfloat16)
    down_grad = down_term.astype(jnp.bfloat16)
    return (outputs[None], input_grads[None], gate_grad[None], up_grad[None], down_grad[None])


def solution(mesh):
    placed = (
        P("expert", "dp", None),
        P("expert", "dp", None),
        P(),
        P("expert", None, "dp"),
        P("expert", None, "dp"),
        P("expert", "dp", None),
    )
    return jax.shard_map(
        shards,
        mesh=mesh,
        in_specs=placed,
        out_specs=(
            P("expert", "dp", None),
            P("expert", "dp", None),
            P("expert", None, "dp"),
            P("expert", None, "dp"),
            P("expert", "dp", None),
        ),
        check_vma=False,
    )
```

```python
import jax
import jax.numpy as jnp
from jax import lax
from jax.sharding import PartitionSpec as P


def silu_slope(value):
    sigma = jax.nn.sigmoid(value)
    return sigma * (1.0 + value * (1.0 - sigma))


def contract_last(left, right):
    return lax.dot_general(
        left, right, (((1,), (1,)), ((), ())), preferred_element_type=jnp.float32
    )


def contract_first(left, right):
    return lax.dot_general(
        left, right, (((0,), (0,)), ((), ())), preferred_element_type=jnp.float32
    )


def expert_work(rows, cot_rows, gate_w, up_w, down_w):
    gate = jnp.dot(rows, gate_w, preferred_element_type=jnp.float32)
    up = jnp.dot(rows, up_w, preferred_element_type=jnp.float32)
    active = jax.nn.silu(gate)
    hidden = (active * up).astype(jnp.bfloat16)
    out_part = jnp.dot(hidden, down_w, preferred_element_type=jnp.float32).astype(jnp.bfloat16)
    out_part, hidden, gate, up = lax.optimization_barrier((out_part, hidden, gate, up))
    active = jax.nn.silu(gate)
    hidden_grad = contract_last(cot_rows, down_w)
    gate_act = (hidden_grad * up * silu_slope(gate)).astype(jnp.bfloat16)
    up_act = (hidden_grad * active).astype(jnp.bfloat16)
    in_part = contract_last(gate_act, gate_w) + contract_last(up_act, up_w)
    gate_term = contract_first(rows, gate_act)
    up_term = contract_first(rows, up_act)
    down_term = contract_first(hidden, cot_rows)
    return (out_part, in_part, gate_term, up_term, down_term)


def shards(tokens, cotangent, counts, w_gate, w_up, w_down):
    rows_in = tokens[0]
    cot_in = cotangent[0]
    gate_w = w_gate[0]
    up_w = w_up[0]
    down_w = w_down[0]
    expert_pos = lax.axis_index("expert")
    batch_pos = lax.axis_index("dp")
    expert_ids = jnp.arange(counts.shape[0], dtype=jnp.int32)
    batch_ids = jnp.arange(counts.shape[1], dtype=jnp.int32)
    own_counts = jnp.sum(jnp.where(expert_ids[:, None] == expert_pos, counts, 0), axis=0)
    own_total = jnp.sum(jnp.where(batch_ids == batch_pos, own_counts, 0))
    slots = rows_in.shape[0]
    valid = (jnp.arange(slots, dtype=jnp.int32) < own_total)[:, None]
    masked = jnp.where(valid, rows_in, jnp.zeros_like(rows_in))
    masked_cot = jnp.where(valid, cot_in, jnp.zeros_like(cot_in))
    all_rows = lax.all_gather(masked, "dp", axis=0, tiled=True)
    all_cot = lax.all_gather(masked_cot, "dp", axis=0, tiled=True)
    out_part, in_part, gate_term, up_term, down_term = expert_work(
        all_rows, all_cot, gate_w, up_w, down_w
    )
    groups = lax.axis_size("dp")
    outputs = lax.psum_scatter(
        out_part.reshape(groups, slots, -1), "dp", scatter_dimension=0, tiled=False
    )
    input_grads = lax.psum_scatter(
        in_part.astype(jnp.bfloat16).reshape(groups, slots, -1), "dp", scatter_dimension=0, tiled=False
    )
    gate_grad = gate_term.astype(jnp.bfloat16)
    up_grad = up_term.astype(jnp.bfloat16)
    down_grad = down_term.astype(jnp.bfloat16)
    return (outputs[None], input_grads[None], gate_grad[None], up_grad[None], down_grad[None])


def solution(mesh):
    placed = (
        P("expert", "dp", None),
        P("expert", "dp", None),
        P(),
        P("expert", None, "dp"),
        P("expert", None, "dp"),
        P("expert", "dp", None),
    )
    return jax.shard_map(
        shards,
        mesh=mesh,
        in_specs=placed,
        out_specs=(
            P("expert", "dp", None),
            P("expert", "dp", None),
            P("expert", None, "dp"),
            P("expert", None, "dp"),
            P("expert", "dp", None),
        ),
        check_vma=False,
    )
```

```python
import jax
import jax.numpy as jnp
from jax import lax
from jax.sharding import Mesh, PartitionSpec as P


def silu_slope(value):
    sigma = jax.nn.sigmoid(value)
    return sigma * (1.0 + value * (1.0 - sigma))


def contract_last(left, right):
    return lax.dot_general(
        left, right, (((1,), (1,)), ((), ())), preferred_element_type=jnp.float32
    )


def contract_first(left, right):
    return lax.dot_general(
        left, right, (((0,), (0,)), ((), ())), preferred_element_type=jnp.float32
    )


def expert_work(rows, cot_rows, gate_w, up_w, down_w):
    gate = jnp.dot(rows, gate_w, preferred_element_type=jnp.float32)
    up = jnp.dot(rows, up_w, preferred_element_type=jnp.float32)
    active = jax.nn.silu(gate)
    hidden = (active * up).astype(jnp.bfloat16)
    out_part = jnp.dot(hidden, down_w, preferred_element_type=jnp.float32).astype(jnp.bfloat16)
    out_part, hidden, gate, up = lax.optimization_barrier((out_part, hidden, gate, up))
    active = jax.nn.silu(gate)
    hidden_grad = contract_last(cot_rows, down_w)
    gate_act = (hidden_grad * up * silu_slope(gate)).astype(jnp.bfloat16)
    up_act = (hidden_grad * active).astype(jnp.bfloat16)
    in_part = contract_last(gate_act, gate_w) + contract_last(up_act, up_w)
    gate_term = contract_first(rows, gate_act)
    up_term = contract_first(rows, up_act)
    down_term = contract_first(hidden, cot_rows)
    return (out_part, in_part, gate_term, up_term, down_term)


def y_shift(value, distance):
    size = lax.axis_size("y")
    return lax.ppermute(value, "y", [(i, (i + distance) % size) for i in range(size)])


def core_swap(value):
    return lax.ppermute(value, "core", [(0, 1), (1, 0)])


def gather_rows(block):
    cut = block.shape[0] // 2 // 8 * 8 + 8
    from_prev = y_shift(block, 1)
    from_next = y_shift(block, -1)
    far = jnp.concatenate([y_shift(from_prev[:cut], 1), y_shift(from_next[cut:], -1)], axis=0)
    mine = jnp.concatenate([block, from_prev, from_next, far], axis=0)
    return jnp.concatenate([mine, core_swap(mine)], axis=0)


def scatter_rows(parts):
    half = parts.shape[0] // 2
    slots = half // 4
    cut = slots // 2 // 8 * 8 + 8
    acc = parts[:half].astype(jnp.float32) + core_swap(parts[half:]).astype(jnp.float32)
    own, prev, nxt, far = (acc[k * slots:(k + 1) * slots] for k in range(4))
    prev = prev + jnp.pad(
        y_shift(far[:cut].astype(jnp.bfloat16), -1).astype(jnp.float32), ((0, slots - cut), (0, 0))
    )
    nxt = nxt + jnp.pad(
        y_shift(far[cut:].astype(jnp.bfloat16), 1).astype(jnp.float32), ((cut, 0), (0, 0))
    )
    total = (
        own
        + y_shift(prev.astype(jnp.bfloat16), -1).astype(jnp.float32)
        + y_shift(nxt.astype(jnp.bfloat16), 1).astype(jnp.float32)
    )
    return total.astype(jnp.bfloat16)


def shards(tokens, cotangent, counts, w_gate, w_up, w_down):
    rows_in = tokens[0]
    cot_in = cotangent[0]
    gate_w = w_gate[0]
    up_w = w_up[0]
    down_w = w_down[0]
    expert_pos = lax.axis_index("expert")
    batch_pos = lax.axis_index("y") * lax.axis_size("core") + lax.axis_index("core")
    expert_ids = jnp.arange(counts.shape[0], dtype=jnp.int32)
    batch_ids = jnp.arange(counts.shape[1], dtype=jnp.int32)
    own_counts = jnp.sum(jnp.where(expert_ids[:, None] == expert_pos, counts, 0), axis=0)
    own_total = jnp.sum(jnp.where(batch_ids == batch_pos, own_counts, 0))
    slots = rows_in.shape[0]
    valid = (jnp.arange(slots, dtype=jnp.int32) < own_total)[:, None]
    masked = jnp.where(valid, rows_in, jnp.zeros_like(rows_in))
    masked_cot = jnp.where(valid, cot_in, jnp.zeros_like(cot_in))
    all_rows = gather_rows(masked)
    all_cot = gather_rows(masked_cot)
    out_part, in_part, gate_term, up_term, down_term = expert_work(
        all_rows, all_cot, gate_w, up_w, down_w
    )
    outputs = scatter_rows(out_part)
    input_grads = scatter_rows(in_part.astype(jnp.bfloat16))
    gate_grad = gate_term.astype(jnp.bfloat16)
    up_grad = up_term.astype(jnp.bfloat16)
    down_grad = down_term.astype(jnp.bfloat16)
    return (outputs[None], input_grads[None], gate_grad[None], up_grad[None], down_grad[None])


def solution(mesh):
    chips = mesh.shape["dp"] // 2
    split = Mesh(mesh.devices.reshape(mesh.shape["expert"], chips, 2), ("expert", "y", "core"))
    rows = P("expert", ("y", "core"), None)
    cols = P("expert", None, ("y", "core"))
    return jax.shard_map(
        shards,
        mesh=split,
        in_specs=(rows, rows, P(), cols, cols, rows),
        out_specs=(rows, rows, cols, cols, rows),
        check_vma=False,
    )
```

```python
import jax
import jax.numpy as jnp
from jax import lax
from jax.sharding import Mesh, PartitionSpec as P


def silu_slope(value):
    sigma = jax.nn.sigmoid(value)
    return sigma * (1.0 + value * (1.0 - sigma))


def contract_last(left, right):
    return lax.dot_general(
        left, right, (((1,), (1,)), ((), ())), preferred_element_type=jnp.float32
    )


def contract_first(left, right):
    return lax.dot_general(
        left, right, (((0,), (0,)), ((), ())), preferred_element_type=jnp.float32
    )


def expert_work(rows, cot_rows, gate_w, up_w, down_w):
    gate = jnp.dot(rows, gate_w, preferred_element_type=jnp.float32)
    up = jnp.dot(rows, up_w, preferred_element_type=jnp.float32)
    active = jax.nn.silu(gate)
    hidden = (active * up).astype(jnp.bfloat16)
    out_part = jnp.dot(hidden, down_w, preferred_element_type=jnp.float32).astype(jnp.bfloat16)
    out_part, hidden, gate, up = lax.optimization_barrier((out_part, hidden, gate, up))
    active = jax.nn.silu(gate)
    hidden_grad = contract_last(cot_rows, down_w)
    gate_act = (hidden_grad * up * silu_slope(gate)).astype(jnp.bfloat16)
    up_act = (hidden_grad * active).astype(jnp.bfloat16)
    in_part = contract_last(gate_act, gate_w) + contract_last(up_act, up_w)
    gate_term = contract_first(rows, gate_act)
    up_term = contract_first(rows, up_act)
    down_term = contract_first(hidden, cot_rows)
    return (out_part, in_part, gate_term, up_term, down_term)


def y_shift(value, distance):
    size = lax.axis_size("y")
    return lax.ppermute(value, "y", [(i, (i + distance) % size) for i in range(size)])


def core_swap(value):
    return lax.ppermute(value, "core", [(0, 1), (1, 0)])


def gather_rows(block):
    cut = block.shape[0] // 2
    from_prev = y_shift(block, 1)
    from_next = y_shift(block, -1)
    far = jnp.concatenate([y_shift(from_prev[:cut], 1), y_shift(from_next[cut:], -1)], axis=0)
    mine = jnp.concatenate([block, from_prev, from_next, far], axis=0)
    return jnp.concatenate([mine, core_swap(mine)], axis=0)


def scatter_rows(parts):
    half = parts.shape[0] // 2
    slots = half // 4
    cut = slots // 2
    acc = parts[:half].astype(jnp.float32) + core_swap(parts[half:]).astype(jnp.float32)
    own, prev, nxt, far = (acc[k * slots:(k + 1) * slots] for k in range(4))
    prev = prev + jnp.pad(
        y_shift(far[:cut].astype(jnp.bfloat16), -1).astype(jnp.float32), ((0, slots - cut), (0, 0))
    )
    nxt = nxt + jnp.pad(
        y_shift(far[cut:].astype(jnp.bfloat16), 1).astype(jnp.float32), ((cut, 0), (0, 0))
    )
    total = (
        own
        + y_shift(prev.astype(jnp.bfloat16), -1).astype(jnp.float32)
        + y_shift(nxt.astype(jnp.bfloat16), 1).astype(jnp.float32)
    )
    return total.astype(jnp.bfloat16)


def shards(tokens, cotangent, counts, w_gate, w_up, w_down):
    rows_in = tokens[0]
    cot_in = cotangent[0]
    gate_w = w_gate[0]
    up_w = w_up[0]
    down_w = w_down[0]
    expert_pos = lax.axis_index("expert")
    batch_pos = lax.axis_index("y") * lax.axis_size("core") + lax.axis_index("core")
    expert_ids = jnp.arange(counts.shape[0], dtype=jnp.int32)
    batch_ids = jnp.arange(counts.shape[1], dtype=jnp.int32)
    own_counts = jnp.sum(jnp.where(expert_ids[:, None] == expert_pos, counts, 0), axis=0)
    own_total = jnp.sum(jnp.where(batch_ids == batch_pos, own_counts, 0))
    slots = rows_in.shape[0]
    padded = -(-slots // 16) * 16
    valid = (jnp.arange(padded, dtype=jnp.int32) < jnp.minimum(own_total, slots))[:, None]
    grow = ((0, padded - slots), (0, 0))
    masked = jnp.where(valid, jnp.pad(rows_in, grow), 0).astype(rows_in.dtype)
    masked_cot = jnp.where(valid, jnp.pad(cot_in, grow), 0).astype(cot_in.dtype)
    all_rows = gather_rows(masked)
    all_cot = gather_rows(masked_cot)
    out_part, in_part, gate_term, up_term, down_term = expert_work(
        all_rows, all_cot, gate_w, up_w, down_w
    )
    outputs = scatter_rows(out_part)[:slots]
    input_grads = scatter_rows(in_part.astype(jnp.bfloat16))[:slots]
    gate_grad = gate_term.astype(jnp.bfloat16)
    up_grad = up_term.astype(jnp.bfloat16)
    down_grad = down_term.astype(jnp.bfloat16)
    return (outputs[None], input_grads[None], gate_grad[None], up_grad[None], down_grad[None])


def solution(mesh):
    chips = mesh.shape["dp"] // 2
    split = Mesh(mesh.devices.reshape(mesh.shape["expert"], chips, 2), ("expert", "y", "core"))
    rows = P("expert", ("y", "core"), None)
    cols = P("expert", None, ("y", "core"))
    return jax.shard_map(
        shards,
        mesh=split,
        in_specs=(rows, rows, P(), cols, cols, rows),
        out_specs=(rows, rows, cols, cols, rows),
        check_vma=False,
    )
```

```python
import jax
import jax.numpy as jnp
from jax import lax
from jax.sharding import Mesh, PartitionSpec as P


def silu_slope(value):
    sigma = jax.nn.sigmoid(value)
    return sigma * (1.0 + value * (1.0 - sigma))


def contract_last(left, right):
    return lax.dot_general(
        left, right, (((1,), (1,)), ((), ())), preferred_element_type=jnp.float32
    )


def contract_first(left, right):
    return lax.dot_general(
        left, right, (((0,), (0,)), ((), ())), preferred_element_type=jnp.float32
    )


def expert_work(rows, cot_rows, gate_w, up_w, down_w):
    gate = jnp.dot(rows, gate_w, preferred_element_type=jnp.float32)
    up = jnp.dot(rows, up_w, preferred_element_type=jnp.float32)
    active = jax.nn.silu(gate)
    hidden = (active * up).astype(jnp.bfloat16)
    out_part = jnp.dot(hidden, down_w, preferred_element_type=jnp.float32).astype(jnp.bfloat16)
    out_part, hidden, gate, up = lax.optimization_barrier((out_part, hidden, gate, up))
    active = jax.nn.silu(gate)
    hidden_grad = contract_last(cot_rows, down_w)
    gate_act = (hidden_grad * up * silu_slope(gate)).astype(jnp.bfloat16)
    up_act = (hidden_grad * active).astype(jnp.bfloat16)
    in_part = contract_last(gate_act, gate_w) + contract_last(up_act, up_w)
    gate_term = contract_first(rows, gate_act)
    up_term = contract_first(rows, up_act)
    down_term = contract_first(hidden, cot_rows)
    return (out_part, in_part, gate_term, up_term, down_term)


def y_shift(value, distance):
    size = lax.axis_size("y")
    return lax.ppermute(value, "y", [(i, (i + distance) % size) for i in range(size)])


def core_swap(value):
    return lax.ppermute(value, "core", [(0, 1), (1, 0)])


def gather_rows(block, after=()):
    cut = block.shape[0] // 2
    block, _ = lax.optimization_barrier((block, after))
    from_prev = y_shift(block, 1)
    from_next = y_shift(block, -1)
    far = jnp.concatenate([y_shift(from_prev[:cut], 1), y_shift(from_next[cut:], -1)], axis=0)
    mine = jnp.concatenate([block, from_prev, from_next, far], axis=0)
    return jnp.concatenate([mine, core_swap(mine)], axis=0), (from_prev, from_next)


def scatter_rows(parts):
    half = parts.shape[0] // 2
    slots = half // 4
    cut = slots // 2
    acc = parts[:half].astype(jnp.float32) + core_swap(parts[half:]).astype(jnp.float32)
    own, prev, nxt, far = (acc[k * slots:(k + 1) * slots] for k in range(4))
    prev = prev + jnp.pad(
        y_shift(far[:cut].astype(jnp.bfloat16), -1).astype(jnp.float32), ((0, slots - cut), (0, 0))
    )
    nxt = nxt + jnp.pad(
        y_shift(far[cut:].astype(jnp.bfloat16), 1).astype(jnp.float32), ((cut, 0), (0, 0))
    )
    total = (
        own
        + y_shift(prev.astype(jnp.bfloat16), -1).astype(jnp.float32)
        + y_shift(nxt.astype(jnp.bfloat16), 1).astype(jnp.float32)
    )
    return total.astype(jnp.bfloat16)


def shards(tokens, cotangent, counts, w_gate, w_up, w_down):
    rows_in = tokens[0]
    cot_in = cotangent[0]
    gate_w = w_gate[0]
    up_w = w_up[0]
    down_w = w_down[0]
    expert_pos = lax.axis_index("expert")
    batch_pos = lax.axis_index("y") * lax.axis_size("core") + lax.axis_index("core")
    expert_ids = jnp.arange(counts.shape[0], dtype=jnp.int32)
    batch_ids = jnp.arange(counts.shape[1], dtype=jnp.int32)
    own_counts = jnp.sum(jnp.where(expert_ids[:, None] == expert_pos, counts, 0), axis=0)
    own_total = jnp.sum(jnp.where(batch_ids == batch_pos, own_counts, 0))
    slots = rows_in.shape[0]
    padded = -(-slots // 16) * 16
    valid = (jnp.arange(padded, dtype=jnp.int32) < jnp.minimum(own_total, slots))[:, None]
    grow = ((0, padded - slots), (0, 0))
    masked = jnp.where(valid, jnp.pad(rows_in, grow), 0).astype(rows_in.dtype)
    masked_cot = jnp.where(valid, jnp.pad(cot_in, grow), 0).astype(cot_in.dtype)
    all_rows, first_hop = gather_rows(masked)
    all_cot, _ = gather_rows(masked_cot, first_hop)
    out_part, in_part, gate_term, up_term, down_term = expert_work(
        all_rows, all_cot, gate_w, up_w, down_w
    )
    outputs = scatter_rows(out_part)[:slots]
    input_grads = scatter_rows(in_part.astype(jnp.bfloat16))[:slots]
    gate_grad = gate_term.astype(jnp.bfloat16)
    up_grad = up_term.astype(jnp.bfloat16)
    down_grad = down_term.astype(jnp.bfloat16)
    return (outputs[None], input_grads[None], gate_grad[None], up_grad[None], down_grad[None])


def solution(mesh):
    chips = mesh.shape["dp"] // 2
    split = Mesh(mesh.devices.reshape(mesh.shape["expert"], chips, 2), ("expert", "y", "core"))
    rows = P("expert", ("y", "core"), None)
    cols = P("expert", None, ("y", "core"))

    return jax.shard_map(
        shards,
        mesh=split,
        in_specs=(rows, rows, P(), cols, cols, rows),
        out_specs=(rows, rows, cols, cols, rows),
        check_vma=False,
    )
```

```python
import jax
import jax.numpy as jnp
from jax import lax
from jax.sharding import Mesh, PartitionSpec as P


def silu_slope(value):
    sigma = jax.nn.sigmoid(value)
    return sigma * (1.0 + value * (1.0 - sigma))


def contract_last(left, right):
    return lax.dot_general(
        left, right, (((1,), (1,)), ((), ())), preferred_element_type=jnp.float32
    )


def contract_first(left, right):
    return lax.dot_general(
        left, right, (((0,), (0,)), ((), ())), preferred_element_type=jnp.float32
    )


def expert_work(rows, cot_rows, gate_w, up_w, down_w):
    gate = jnp.dot(rows, gate_w, preferred_element_type=jnp.float32)
    up = jnp.dot(rows, up_w, preferred_element_type=jnp.float32)
    active = jax.nn.silu(gate)
    hidden = (active * up).astype(jnp.bfloat16)
    out_part = jnp.dot(hidden, down_w, preferred_element_type=jnp.float32).astype(jnp.bfloat16)
    out_part, hidden, gate, up = lax.optimization_barrier((out_part, hidden, gate, up))
    active = jax.nn.silu(gate)
    hidden_grad = contract_last(cot_rows, down_w)
    gate_act = (hidden_grad * up * silu_slope(gate)).astype(jnp.bfloat16)
    up_act = (hidden_grad * active).astype(jnp.bfloat16)
    in_part = contract_last(gate_act, gate_w) + contract_last(up_act, up_w)
    gate_term = contract_first(rows, gate_act)
    up_term = contract_first(rows, up_act)
    down_term = contract_first(hidden, cot_rows)
    return (out_part, in_part, gate_term, up_term, down_term)


def y_shift(value, distance):
    size = lax.axis_size("y")
    return lax.ppermute(value, "y", [(i, (i + distance) % size) for i in range(size)])


def core_swap(value):
    return lax.ppermute(value, "core", [(0, 1), (1, 0)])


def gather_rows(block, after=()):
    cut = block.shape[0] // 2
    block, _ = lax.optimization_barrier((block, after))
    from_prev = y_shift(block, 1)
    from_next = y_shift(block, -1)
    far = jnp.concatenate([y_shift(from_prev[:cut], 1), y_shift(from_next[cut:], -1)], axis=0)
    mine = jnp.concatenate([block, from_prev, from_next, far], axis=0)
    return jnp.concatenate([mine, core_swap(mine)], axis=0), (from_prev, from_next)


def scatter_rows(parts):
    half = parts.shape[0] // 2
    slots = half // 4
    cut = slots // 2
    acc = parts[:half].astype(jnp.float32) + core_swap(parts[half:]).astype(jnp.float32)
    own, prev, nxt, far = (acc[k * slots:(k + 1) * slots] for k in range(4))
    back_prev = y_shift(far[:cut].astype(jnp.bfloat16), -1)
    back_next = y_shift(far[cut:].astype(jnp.bfloat16), 1)
    prev = prev + jnp.pad(back_prev.astype(jnp.float32), ((0, slots - cut), (0, 0)))
    nxt = nxt + jnp.pad(back_next.astype(jnp.float32), ((cut, 0), (0, 0)))
    from_next = y_shift(prev.astype(jnp.bfloat16), -1)
    from_prev = y_shift(nxt.astype(jnp.bfloat16), 1)
    total = own + from_next.astype(jnp.float32) + from_prev.astype(jnp.float32)
    return total.astype(jnp.bfloat16)


def shards(tokens, cotangent, counts, w_gate, w_up, w_down):
    rows_in = tokens[0]
    cot_in = cotangent[0]
    gate_w = w_gate[0]
    up_w = w_up[0]
    down_w = w_down[0]
    expert_pos = lax.axis_index("expert")
    batch_pos = lax.axis_index("y") * lax.axis_size("core") + lax.axis_index("core")
    expert_ids = jnp.arange(counts.shape[0], dtype=jnp.int32)
    batch_ids = jnp.arange(counts.shape[1], dtype=jnp.int32)
    own_counts = jnp.sum(jnp.where(expert_ids[:, None] == expert_pos, counts, 0), axis=0)
    own_total = jnp.sum(jnp.where(batch_ids == batch_pos, own_counts, 0))
    slots = rows_in.shape[0]
    padded = -(-slots // 16) * 16
    valid = (jnp.arange(padded, dtype=jnp.int32) < jnp.minimum(own_total, slots))[:, None]
    grow = ((0, padded - slots), (0, 0))
    masked = jnp.where(valid, jnp.pad(rows_in, grow), 0).astype(rows_in.dtype)
    masked_cot = jnp.where(valid, jnp.pad(cot_in, grow), 0).astype(cot_in.dtype)
    all_rows, first_hop = gather_rows(masked)
    all_cot, _ = gather_rows(masked_cot, first_hop)
    out_part, in_part, gate_term, up_term, down_term = expert_work(
        all_rows, all_cot, gate_w, up_w, down_w
    )
    outputs = scatter_rows(out_part)[:slots]
    input_grads = scatter_rows(in_part.astype(jnp.bfloat16))[:slots]
    gate_grad = gate_term.astype(jnp.bfloat16)
    up_grad = up_term.astype(jnp.bfloat16)
    down_grad = down_term.astype(jnp.bfloat16)
    return (outputs[None], input_grads[None], gate_grad[None], up_grad[None], down_grad[None])


def solution(mesh):
    chips = mesh.shape["dp"] // 2
    split = Mesh(mesh.devices.reshape(mesh.shape["expert"], chips, 2), ("expert", "y", "core"))
    rows = P("expert", ("y", "core"), None)
    cols = P("expert", None, ("y", "core"))

    return jax.shard_map(
        shards,
        mesh=split,
        in_specs=(rows, rows, P(), cols, cols, rows),
        out_specs=(rows, rows, cols, cols, rows),
        check_vma=False,
    )
```

```python
import jax
import jax.numpy as jnp
from jax import lax
from jax.sharding import Mesh, PartitionSpec as P


def silu_slope(value):
    sigma = jax.nn.sigmoid(value)
    return sigma * (1.0 + value * (1.0 - sigma))


def contract_last(left, right):
    return lax.dot_general(
        left, right, (((1,), (1,)), ((), ())), preferred_element_type=jnp.float32
    )


def contract_first(left, right):
    return lax.dot_general(
        left, right, (((0,), (0,)), ((), ())), preferred_element_type=jnp.float32
    )


def expert_work(rows, cot_rows, gate_w, up_w, down_w):
    gate = jnp.dot(rows, gate_w, preferred_element_type=jnp.float32)
    up = jnp.dot(rows, up_w, preferred_element_type=jnp.float32)
    active = jax.nn.silu(gate)
    hidden = (active * up).astype(jnp.bfloat16)
    out_part = jnp.dot(hidden, down_w, preferred_element_type=jnp.float32).astype(jnp.bfloat16)
    out_part, hidden, gate, up = lax.optimization_barrier((out_part, hidden, gate, up))
    active = jax.nn.silu(gate)
    hidden_grad = contract_last(cot_rows, down_w)
    gate_act = (hidden_grad * up * silu_slope(gate)).astype(jnp.bfloat16)
    up_act = (hidden_grad * active).astype(jnp.bfloat16)
    in_part = contract_last(gate_act, gate_w) + contract_last(up_act, up_w)
    gate_term = contract_first(rows, gate_act)
    up_term = contract_first(rows, up_act)
    down_term = contract_first(hidden, cot_rows)
    return (out_part, in_part, gate_term, up_term, down_term)


def y_shift(value, distance):
    size = lax.axis_size("y")
    return lax.ppermute(value, "y", [(i, (i + distance) % size) for i in range(size)])


def core_swap(value):
    return lax.ppermute(value, "core", [(0, 1), (1, 0)])


def scatter_rows(parts):
    half = parts.shape[0] // 2
    slots = half // 4
    cut = slots // 2
    acc = parts[:half].astype(jnp.float32) + core_swap(parts[half:]).astype(jnp.float32)
    own, prev, nxt, far = (acc[k * slots:(k + 1) * slots] for k in range(4))
    back_prev = y_shift(far[:cut].astype(jnp.bfloat16), -1)
    back_next = y_shift(far[cut:].astype(jnp.bfloat16), 1)
    prev = prev + jnp.pad(back_prev.astype(jnp.float32), ((0, slots - cut), (0, 0)))
    nxt = nxt + jnp.pad(back_next.astype(jnp.float32), ((cut, 0), (0, 0)))
    from_next = y_shift(prev.astype(jnp.bfloat16), -1)
    from_prev = y_shift(nxt.astype(jnp.bfloat16), 1)
    total = own + from_next.astype(jnp.float32) + from_prev.astype(jnp.float32)
    return total.astype(jnp.bfloat16)


def shards(tokens, cotangent, counts, w_gate, w_up, w_down):
    rows_in = tokens[0]
    cot_in = cotangent[0]
    gate_w = w_gate[0]
    up_w = w_up[0]
    down_w = w_down[0]
    expert_pos = lax.axis_index("expert")
    batch_pos = lax.axis_index("y") * lax.axis_size("core") + lax.axis_index("core")
    expert_ids = jnp.arange(counts.shape[0], dtype=jnp.int32)
    batch_ids = jnp.arange(counts.shape[1], dtype=jnp.int32)
    own_counts = jnp.sum(jnp.where(expert_ids[:, None] == expert_pos, counts, 0), axis=0)
    own_total = jnp.sum(jnp.where(batch_ids == batch_pos, own_counts, 0))
    slots = rows_in.shape[0]
    padded = -(-slots // 16) * 16
    valid = (jnp.arange(padded, dtype=jnp.int32) < jnp.minimum(own_total, slots))[:, None]
    grow = ((0, padded - slots), (0, 0))
    masked = jnp.where(valid, jnp.pad(rows_in, grow), 0).astype(rows_in.dtype)
    masked_cot = jnp.where(valid, jnp.pad(cot_in, grow), 0).astype(cot_in.dtype)
    cut = masked.shape[0] // 2
    tok_prev = y_shift(masked, 1)
    tok_next = y_shift(masked, -1)
    got_prev = y_shift(jnp.concatenate([tok_prev[:cut], masked_cot], axis=0), 1)
    got_next = y_shift(jnp.concatenate([tok_next[cut:], masked_cot], axis=0), -1)
    tok_far_a, cot_prev = got_prev[:cut], got_prev[cut:]
    tok_far_b, cot_next = got_next[:cut], got_next[cut:]
    tok_mine = jnp.concatenate([masked, tok_prev, tok_next, tok_far_a, tok_far_b], axis=0)
    all_rows = jnp.concatenate([tok_mine, core_swap(tok_mine)], axis=0)
    cot_far = jnp.concatenate([y_shift(cot_prev[:cut], 1), y_shift(cot_next[cut:], -1)], axis=0)
    cot_mine = jnp.concatenate([masked_cot, cot_prev, cot_next, cot_far], axis=0)
    all_cot = jnp.concatenate([cot_mine, core_swap(cot_mine)], axis=0)
    out_part, in_part, gate_term, up_term, down_term = expert_work(
        all_rows, all_cot, gate_w, up_w, down_w
    )
    outputs = scatter_rows(out_part)[:slots]
    input_grads = scatter_rows(in_part.astype(jnp.bfloat16))[:slots]
    gate_grad = gate_term.astype(jnp.bfloat16)
    up_grad = up_term.astype(jnp.bfloat16)
    down_grad = down_term.astype(jnp.bfloat16)
    return (outputs[None], input_grads[None], gate_grad[None], up_grad[None], down_grad[None])


def solution(mesh):
    chips = mesh.shape["dp"] // 2
    split = Mesh(mesh.devices.reshape(mesh.shape["expert"], chips, 2), ("expert", "y", "core"))
    rows = P("expert", ("y", "core"), None)
    cols = P("expert", None, ("y", "core"))

    return jax.shard_map(
        shards,
        mesh=split,
        in_specs=(rows, rows, P(), cols, cols, rows),
        out_specs=(rows, rows, cols, cols, rows),
        check_vma=False,
    )
```

```python
import jax
import jax.numpy as jnp
from jax import lax
from jax.sharding import Mesh, PartitionSpec as P


def silu_slope(value):
    sigma = jax.nn.sigmoid(value)
    return sigma * (1.0 + value * (1.0 - sigma))


def contract_last(left, right):
    return lax.dot_general(
        left, right, (((1,), (1,)), ((), ())), preferred_element_type=jnp.float32
    )


def contract_first(left, right):
    return lax.dot_general(
        left, right, (((0,), (0,)), ((), ())), preferred_element_type=jnp.float32
    )


def expert_work(rows, cot_rows, gate_w, up_w, down_w):
    gate = jnp.dot(rows, gate_w, preferred_element_type=jnp.float32)
    up = jnp.dot(rows, up_w, preferred_element_type=jnp.float32)
    active = jax.nn.silu(gate)
    hidden = (active * up).astype(jnp.bfloat16)
    out_part = jnp.dot(hidden, down_w, preferred_element_type=jnp.float32).astype(jnp.bfloat16)
    out_part, hidden, gate, up = lax.optimization_barrier((out_part, hidden, gate, up))
    active = jax.nn.silu(gate)
    hidden_grad = contract_last(cot_rows, down_w)
    gate_act = (hidden_grad * up * silu_slope(gate)).astype(jnp.bfloat16)
    up_act = (hidden_grad * active).astype(jnp.bfloat16)
    half = rows.shape[0] // 2
    in_part = tuple(
        (
            contract_last(gate_act[pick], gate_w) + contract_last(up_act[pick], up_w)
        ).astype(jnp.bfloat16)
        for pick in (slice(half, None), slice(None, half))
    )
    gate_term = contract_first(rows, gate_act)
    up_term = contract_first(rows, up_act)
    down_term = contract_first(hidden, cot_rows)
    return (out_part, in_part, gate_term, up_term, down_term)


def y_shift(value, distance):
    size = lax.axis_size("y")
    return lax.ppermute(value, "y", [(i, (i + distance) % size) for i in range(size)])


def core_swap(value):
    return lax.ppermute(value, "core", [(0, 1), (1, 0)])


def scatter_rows(other, mine):
    slots = mine.shape[0] // 4
    cut = slots // 2
    got = core_swap(other)
    own, prev, nxt, far = (
        mine[k * slots:(k + 1) * slots].astype(jnp.float32)
        + got[k * slots:(k + 1) * slots].astype(jnp.float32)
        for k in range(4)
    )
    back_prev = y_shift(far[:cut].astype(jnp.bfloat16), -1)
    back_next = y_shift(far[cut:].astype(jnp.bfloat16), 1)
    prev = prev + jnp.pad(back_prev.astype(jnp.float32), ((0, slots - cut), (0, 0)))
    nxt = nxt + jnp.pad(back_next.astype(jnp.float32), ((cut, 0), (0, 0)))
    from_next = y_shift(prev.astype(jnp.bfloat16), -1)
    from_prev = y_shift(nxt.astype(jnp.bfloat16), 1)
    total = own + from_next.astype(jnp.float32) + from_prev.astype(jnp.float32)
    return total.astype(jnp.bfloat16)


def shards(tokens, cotangent, counts, w_gate, w_up, w_down):
    rows_in = tokens[0]
    cot_in = cotangent[0]
    gate_w = w_gate[0]
    up_w = w_up[0]
    down_w = w_down[0]
    expert_pos = lax.axis_index("expert")
    batch_pos = lax.axis_index("y") * lax.axis_size("core") + lax.axis_index("core")
    expert_ids = jnp.arange(counts.shape[0], dtype=jnp.int32)
    batch_ids = jnp.arange(counts.shape[1], dtype=jnp.int32)
    own_counts = jnp.sum(jnp.where(expert_ids[:, None] == expert_pos, counts, 0), axis=0)
    own_total = jnp.sum(jnp.where(batch_ids == batch_pos, own_counts, 0))
    slots = rows_in.shape[0]
    padded = -(-slots // 16) * 16
    valid = (jnp.arange(padded, dtype=jnp.int32) < jnp.minimum(own_total, slots))[:, None]
    grow = ((0, padded - slots), (0, 0))
    masked = jnp.where(valid, jnp.pad(rows_in, grow), 0).astype(rows_in.dtype)
    masked_cot = jnp.where(valid, jnp.pad(cot_in, grow), 0).astype(cot_in.dtype)
    cut = masked.shape[0] // 2
    tok_prev = y_shift(masked, 1)
    tok_next = y_shift(masked, -1)
    got_prev = y_shift(jnp.concatenate([tok_prev[:cut], masked_cot], axis=0), 1)
    got_next = y_shift(jnp.concatenate([tok_next[cut:], masked_cot], axis=0), -1)
    tok_far_a, cot_prev = got_prev[:cut], got_prev[cut:]
    tok_far_b, cot_next = got_next[:cut], got_next[cut:]
    tok_mine = jnp.concatenate([masked, tok_prev, tok_next, tok_far_a, tok_far_b], axis=0)
    all_rows = jnp.concatenate([tok_mine, core_swap(tok_mine)], axis=0)
    cot_far = jnp.concatenate([y_shift(cot_prev[:cut], 1), y_shift(cot_next[cut:], -1)], axis=0)
    cot_mine = jnp.concatenate([masked_cot, cot_prev, cot_next, cot_far], axis=0)
    all_cot = jnp.concatenate([cot_mine, core_swap(cot_mine)], axis=0)
    out_part, in_part, gate_term, up_term, down_term = expert_work(
        all_rows, all_cot, gate_w, up_w, down_w
    )
    half = out_part.shape[0] // 2
    outputs = scatter_rows(out_part[half:], out_part[:half])[:slots]
    input_grads = scatter_rows(*in_part)[:slots]
    gate_grad = gate_term.astype(jnp.bfloat16)
    up_grad = up_term.astype(jnp.bfloat16)
    down_grad = down_term.astype(jnp.bfloat16)
    return (outputs[None], input_grads[None], gate_grad[None], up_grad[None], down_grad[None])


def solution(mesh):
    chips = mesh.shape["dp"] // 2
    split = Mesh(mesh.devices.reshape(mesh.shape["expert"], chips, 2), ("expert", "y", "core"))
    rows = P("expert", ("y", "core"), None)
    cols = P("expert", None, ("y", "core"))

    return jax.shard_map(
        shards,
        mesh=split,
        in_specs=(rows, rows, P(), cols, cols, rows),
        out_specs=(rows, rows, cols, cols, rows),
        check_vma=False,
    )
```

```python
import jax
import jax.numpy as jnp
from jax import lax
from jax.sharding import Mesh, PartitionSpec as P


def silu_slope(value):
    sigma = jax.nn.sigmoid(value)
    return sigma * (1.0 + value * (1.0 - sigma))


def contract_last(left, right):
    return lax.dot_general(
        left, right, (((1,), (1,)), ((), ())), preferred_element_type=jnp.float32
    )


def contract_first(left, right):
    return lax.dot_general(
        left, right, (((0,), (0,)), ((), ())), preferred_element_type=jnp.float32
    )


def expert_work(rows, cot_rows, gate_w, up_w, down_w):
    gate = jnp.dot(rows, gate_w, preferred_element_type=jnp.float32)
    up = jnp.dot(rows, up_w, preferred_element_type=jnp.float32)
    active = jax.nn.silu(gate)
    hidden = (active * up).astype(jnp.bfloat16)
    out_part = jnp.dot(hidden, down_w, preferred_element_type=jnp.float32).astype(jnp.bfloat16)
    out_part, hidden, gate, up = lax.optimization_barrier((out_part, hidden, gate, up))
    active = jax.nn.silu(gate)
    hidden_grad = contract_last(cot_rows, down_w)
    gate_act = (hidden_grad * up * silu_slope(gate)).astype(jnp.bfloat16)
    up_act = (hidden_grad * active).astype(jnp.bfloat16)
    half = rows.shape[0] // 2
    in_part = tuple(
        (
            contract_last(gate_act[pick], gate_w) + contract_last(up_act[pick], up_w)
        ).astype(jnp.bfloat16)
        for pick in (slice(half, None), slice(None, half))
    )
    gate_term = contract_first(rows, gate_act)
    up_term = contract_first(rows, up_act)
    down_term = contract_first(hidden, cot_rows)
    return (out_part, in_part, gate_term, up_term, down_term)


def y_shift(value, distance):
    size = lax.axis_size("y")
    return lax.ppermute(value, "y", [(i, (i + distance) % size) for i in range(size)])


def core_swap(value):
    return lax.ppermute(value, "core", [(0, 1), (1, 0)])


def scatter_rows(other, mine, slots):
    block = mine.shape[0] // 4
    cut = block // 2
    got = core_swap(other)
    own, prev, nxt, far = (
        mine[k * block:(k + 1) * block].astype(jnp.float32)
        + got[k * block:(k + 1) * block].astype(jnp.float32)
        for k in range(4)
    )
    back_prev = y_shift(far[:cut].astype(jnp.bfloat16), -1)
    back_next = y_shift(far[cut:slots].astype(jnp.bfloat16), 1)
    prev = prev[:slots] + jnp.pad(back_prev.astype(jnp.float32), ((0, slots - cut), (0, 0)))
    nxt = nxt[:slots] + jnp.pad(back_next.astype(jnp.float32), ((cut, 0), (0, 0)))
    from_next = y_shift(prev.astype(jnp.bfloat16), -1)
    from_prev = y_shift(nxt.astype(jnp.bfloat16), 1)
    total = own[:slots] + from_next.astype(jnp.float32) + from_prev.astype(jnp.float32)
    return total.astype(jnp.bfloat16)


def shards(tokens, cotangent, counts, w_gate, w_up, w_down):
    rows_in = tokens[0]
    cot_in = cotangent[0]
    gate_w = w_gate[0]
    up_w = w_up[0]
    down_w = w_down[0]
    expert_pos = lax.axis_index("expert")
    batch_pos = lax.axis_index("y") * lax.axis_size("core") + lax.axis_index("core")
    expert_ids = jnp.arange(counts.shape[0], dtype=jnp.int32)
    batch_ids = jnp.arange(counts.shape[1], dtype=jnp.int32)
    own_counts = jnp.sum(jnp.where(expert_ids[:, None] == expert_pos, counts, 0), axis=0)
    own_total = jnp.sum(jnp.where(batch_ids == batch_pos, own_counts, 0))
    slots = rows_in.shape[0]
    padded = -(-slots // 16) * 16
    valid = (jnp.arange(padded, dtype=jnp.int32) < jnp.minimum(own_total, slots))[:, None]
    grow = ((0, padded - slots), (0, 0))
    masked = jnp.where(valid, jnp.pad(rows_in, grow), 0).astype(rows_in.dtype)
    masked_cot = jnp.where(valid, jnp.pad(cot_in, grow), 0).astype(cot_in.dtype)
    block = masked.shape[0]
    cut = block // 2
    send_tok = masked[:slots]
    send_cot = masked_cot[:slots]

    def fill(rows):
        return jnp.pad(rows, ((0, block - rows.shape[0]), (0, 0)))

    tok_prev = y_shift(send_tok, 1)
    tok_next = y_shift(send_tok, -1)
    got_prev = y_shift(jnp.concatenate([send_cot, tok_prev[:cut]], axis=0), 1)
    got_next = y_shift(jnp.concatenate([send_cot, tok_next[cut:]], axis=0), -1)
    cot_prev, cot_next = got_prev[:slots], got_next[:slots]
    tok_far = jnp.concatenate([got_prev[slots:], got_next[slots:]], axis=0)
    tok_mine = jnp.concatenate([masked, fill(tok_prev), fill(tok_next), fill(tok_far)], axis=0)
    all_rows = jnp.concatenate([tok_mine, core_swap(tok_mine)], axis=0)
    cot_far = jnp.concatenate([y_shift(cot_prev[:cut], 1), y_shift(cot_next[cut:], -1)], axis=0)
    cot_mine = jnp.concatenate([masked_cot, fill(cot_prev), fill(cot_next), fill(cot_far)], axis=0)
    all_cot = jnp.concatenate([cot_mine, core_swap(cot_mine)], axis=0)
    out_part, in_part, gate_term, up_term, down_term = expert_work(
        all_rows, all_cot, gate_w, up_w, down_w
    )
    half = out_part.shape[0] // 2
    outputs = scatter_rows(out_part[half:], out_part[:half], slots)
    input_grads = scatter_rows(*in_part, slots)
    gate_grad = gate_term.astype(jnp.bfloat16)
    up_grad = up_term.astype(jnp.bfloat16)
    down_grad = down_term.astype(jnp.bfloat16)
    return (outputs[None], input_grads[None], gate_grad[None], up_grad[None], down_grad[None])


def solution(mesh):
    chips = mesh.shape["dp"] // 2
    split = Mesh(mesh.devices.reshape(mesh.shape["expert"], chips, 2), ("expert", "y", "core"))
    rows = P("expert", ("y", "core"), None)
    cols = P("expert", None, ("y", "core"))

    return jax.shard_map(
        shards,
        mesh=split,
        in_specs=(rows, rows, P(), cols, cols, rows),
        out_specs=(rows, rows, cols, cols, rows),
        check_vma=False,
    )
```

```python
import jax
import jax.numpy as jnp
from jax import lax
from jax.sharding import Mesh, PartitionSpec as P


def silu_slope(value):
    sigma = jax.nn.sigmoid(value)
    return sigma * (1.0 + value * (1.0 - sigma))


def contract_last(left, right):
    return lax.dot_general(
        left, right, (((1,), (1,)), ((), ())), preferred_element_type=jnp.float32
    )


def contract_first(left, right):
    return lax.dot_general(
        left, right, (((0,), (0,)), ((), ())), preferred_element_type=jnp.float32
    )


def expert_work(rows, cot_rows, gate_w, up_w, down_w):
    gate = jnp.dot(rows, gate_w, preferred_element_type=jnp.float32)
    up = jnp.dot(rows, up_w, preferred_element_type=jnp.float32)
    active = jax.nn.silu(gate)
    hidden = (active * up).astype(jnp.bfloat16)
    half = rows.shape[0] // 2
    out_part = tuple(
        jnp.dot(hidden[pick], down_w, preferred_element_type=jnp.float32).astype(jnp.bfloat16)
        for pick in (slice(half, None), slice(None, half))
    )
    out_part, hidden, gate, up = lax.optimization_barrier((out_part, hidden, gate, up))
    active = jax.nn.silu(gate)
    hidden_grad = contract_last(cot_rows, down_w)
    gate_act = (hidden_grad * up * silu_slope(gate)).astype(jnp.bfloat16)
    up_act = (hidden_grad * active).astype(jnp.bfloat16)
    half = rows.shape[0] // 2
    in_part = tuple(
        (
            contract_last(gate_act[pick], gate_w) + contract_last(up_act[pick], up_w)
        ).astype(jnp.bfloat16)
        for pick in (slice(half, None), slice(None, half))
    )
    gate_term = contract_first(rows, gate_act)
    up_term = contract_first(rows, up_act)
    down_term = contract_first(hidden, cot_rows)
    return (out_part, in_part, gate_term, up_term, down_term)


def y_shift(value, distance):
    size = lax.axis_size("y")
    return lax.ppermute(value, "y", [(i, (i + distance) % size) for i in range(size)])


def core_swap(value):
    return lax.ppermute(value, "core", [(0, 1), (1, 0)])


def scatter_rows(other, mine):
    slots = mine.shape[0] // 4
    cut = slots // 2
    got = core_swap(other)
    own, prev, nxt, far = (
        mine[k * slots:(k + 1) * slots].astype(jnp.float32)
        + got[k * slots:(k + 1) * slots].astype(jnp.float32)
        for k in range(4)
    )
    back_prev = y_shift(far[:cut].astype(jnp.bfloat16), -1)
    back_next = y_shift(far[cut:].astype(jnp.bfloat16), 1)
    prev = prev + jnp.pad(back_prev.astype(jnp.float32), ((0, slots - cut), (0, 0)))
    nxt = nxt + jnp.pad(back_next.astype(jnp.float32), ((cut, 0), (0, 0)))
    from_next = y_shift(prev.astype(jnp.bfloat16), -1)
    from_prev = y_shift(nxt.astype(jnp.bfloat16), 1)
    total = own + from_next.astype(jnp.float32) + from_prev.astype(jnp.float32)
    return total.astype(jnp.bfloat16)


def shards(tokens, cotangent, counts, w_gate, w_up, w_down):
    rows_in = tokens[0]
    cot_in = cotangent[0]
    gate_w = w_gate[0]
    up_w = w_up[0]
    down_w = w_down[0]
    expert_pos = lax.axis_index("expert")
    batch_pos = lax.axis_index("y") * lax.axis_size("core") + lax.axis_index("core")
    expert_ids = jnp.arange(counts.shape[0], dtype=jnp.int32)
    batch_ids = jnp.arange(counts.shape[1], dtype=jnp.int32)
    own_counts = jnp.sum(jnp.where(expert_ids[:, None] == expert_pos, counts, 0), axis=0)
    own_total = jnp.sum(jnp.where(batch_ids == batch_pos, own_counts, 0))
    slots = rows_in.shape[0]
    padded = -(-slots // 16) * 16
    valid = (jnp.arange(padded, dtype=jnp.int32) < jnp.minimum(own_total, slots))[:, None]
    grow = ((0, padded - slots), (0, 0))
    masked = jnp.where(valid, jnp.pad(rows_in, grow), 0).astype(rows_in.dtype)
    masked_cot = jnp.where(valid, jnp.pad(cot_in, grow), 0).astype(cot_in.dtype)
    cut = masked.shape[0] // 2
    tok_prev = y_shift(masked, 1)
    tok_next = y_shift(masked, -1)
    got_prev = y_shift(jnp.concatenate([tok_prev[:cut], masked_cot], axis=0), 1)
    got_next = y_shift(jnp.concatenate([tok_next[cut:], masked_cot], axis=0), -1)
    tok_far_a, cot_prev = got_prev[:cut], got_prev[cut:]
    tok_far_b, cot_next = got_next[:cut], got_next[cut:]
    tok_mine = jnp.concatenate([masked, tok_prev, tok_next, tok_far_a, tok_far_b], axis=0)
    all_rows = jnp.concatenate([tok_mine, core_swap(tok_mine)], axis=0)
    cot_far = jnp.concatenate([y_shift(cot_prev[:cut], 1), y_shift(cot_next[cut:], -1)], axis=0)
    cot_mine = jnp.concatenate([masked_cot, cot_prev, cot_next, cot_far], axis=0)
    all_cot = jnp.concatenate([cot_mine, core_swap(cot_mine)], axis=0)
    out_part, in_part, gate_term, up_term, down_term = expert_work(
        all_rows, all_cot, gate_w, up_w, down_w
    )
    outputs = scatter_rows(*out_part)[:slots]
    input_grads = scatter_rows(*in_part)[:slots]
    gate_grad = gate_term.astype(jnp.bfloat16)
    up_grad = up_term.astype(jnp.bfloat16)
    down_grad = down_term.astype(jnp.bfloat16)
    return (outputs[None], input_grads[None], gate_grad[None], up_grad[None], down_grad[None])


def solution(mesh):
    chips = mesh.shape["dp"] // 2
    split = Mesh(mesh.devices.reshape(mesh.shape["expert"], chips, 2), ("expert", "y", "core"))
    rows = P("expert", ("y", "core"), None)
    cols = P("expert", None, ("y", "core"))

    return jax.shard_map(
        shards,
        mesh=split,
        in_specs=(rows, rows, P(), cols, cols, rows),
        out_specs=(rows, rows, cols, cols, rows),
        check_vma=False,
    )
```

```python
import jax
import jax.numpy as jnp
from jax import lax
from jax.sharding import Mesh, PartitionSpec as P


def silu_slope(value):
    sigma = jax.nn.sigmoid(value)
    return sigma * (1.0 + value * (1.0 - sigma))


def contract_last(left, right):
    return lax.dot_general(
        left, right, (((1,), (1,)), ((), ())), preferred_element_type=jnp.float32
    )


def contract_first(left, right):
    return lax.dot_general(
        left, right, (((0,), (0,)), ((), ())), preferred_element_type=jnp.float32
    )


def expert_work(rows, cot_rows, gate_w, up_w, down_w):
    gate = jnp.dot(rows, gate_w, preferred_element_type=jnp.float32)
    up = jnp.dot(rows, up_w, preferred_element_type=jnp.float32)
    active = jax.nn.silu(gate)
    hidden = (active * up).astype(jnp.bfloat16)
    out_part = jnp.dot(hidden, down_w, preferred_element_type=jnp.float32).astype(jnp.bfloat16)
    out_part, hidden, gate, up = lax.optimization_barrier((out_part, hidden, gate, up))
    active = jax.nn.silu(gate)
    hidden_grad = contract_last(cot_rows, down_w)
    gate_act = (hidden_grad * up * silu_slope(gate)).astype(jnp.bfloat16)
    up_act = (hidden_grad * active).astype(jnp.bfloat16)
    half = rows.shape[0] // 2
    in_part = tuple(
        (
            contract_last(gate_act[pick], gate_w) + contract_last(up_act[pick], up_w)
        ).astype(jnp.bfloat16)
        for pick in (slice(half, None), slice(None, half))
    )
    gate_term = contract_first(rows, gate_act)
    up_term = contract_first(rows, up_act)
    down_term = contract_first(hidden, cot_rows)
    return (out_part, in_part, gate_term, up_term, down_term)


def y_shift(value, distance):
    size = lax.axis_size("y")
    return lax.ppermute(value, "y", [(i, (i + distance) % size) for i in range(size)])


def core_swap(value):
    return lax.ppermute(value, "core", [(0, 1), (1, 0)])


def scatter_rows(other, mine):
    slots = mine.shape[0] // 4
    cut = slots // 2
    got_far = core_swap(other[3 * slots:])
    got = core_swap(other[:3 * slots])
    far = mine[3 * slots:].astype(jnp.float32) + got_far.astype(jnp.float32)
    own, prev, nxt = (
        mine[k * slots:(k + 1) * slots].astype(jnp.float32)
        + got[k * slots:(k + 1) * slots].astype(jnp.float32)
        for k in range(3)
    )
    back_prev = y_shift(far[:cut].astype(jnp.bfloat16), -1)
    back_next = y_shift(far[cut:].astype(jnp.bfloat16), 1)
    prev = prev + jnp.pad(back_prev.astype(jnp.float32), ((0, slots - cut), (0, 0)))
    nxt = nxt + jnp.pad(back_next.astype(jnp.float32), ((cut, 0), (0, 0)))
    from_next = y_shift(prev.astype(jnp.bfloat16), -1)
    from_prev = y_shift(nxt.astype(jnp.bfloat16), 1)
    total = own + from_next.astype(jnp.float32) + from_prev.astype(jnp.float32)
    return total.astype(jnp.bfloat16)


def shards(tokens, cotangent, counts, w_gate, w_up, w_down):
    rows_in = tokens[0]
    cot_in = cotangent[0]
    gate_w = w_gate[0]
    up_w = w_up[0]
    down_w = w_down[0]
    expert_pos = lax.axis_index("expert")
    batch_pos = lax.axis_index("y") * lax.axis_size("core") + lax.axis_index("core")
    expert_ids = jnp.arange(counts.shape[0], dtype=jnp.int32)
    batch_ids = jnp.arange(counts.shape[1], dtype=jnp.int32)
    own_counts = jnp.sum(jnp.where(expert_ids[:, None] == expert_pos, counts, 0), axis=0)
    own_total = jnp.sum(jnp.where(batch_ids == batch_pos, own_counts, 0))
    slots = rows_in.shape[0]
    padded = -(-slots // 16) * 16
    valid = (jnp.arange(padded, dtype=jnp.int32) < jnp.minimum(own_total, slots))[:, None]
    grow = ((0, padded - slots), (0, 0))
    masked = jnp.where(valid, jnp.pad(rows_in, grow), 0).astype(rows_in.dtype)
    masked_cot = jnp.where(valid, jnp.pad(cot_in, grow), 0).astype(cot_in.dtype)
    cut = masked.shape[0] // 2
    tok_prev = y_shift(masked, 1)
    tok_next = y_shift(masked, -1)
    got_prev = y_shift(jnp.concatenate([tok_prev[:cut], masked_cot], axis=0), 1)
    got_next = y_shift(jnp.concatenate([tok_next[cut:], masked_cot], axis=0), -1)
    tok_far_a, cot_prev = got_prev[:cut], got_prev[cut:]
    tok_far_b, cot_next = got_next[:cut], got_next[cut:]
    tok_mine = jnp.concatenate([masked, tok_prev, tok_next, tok_far_a, tok_far_b], axis=0)
    all_rows = jnp.concatenate([tok_mine, core_swap(tok_mine)], axis=0)
    cot_far = jnp.concatenate([y_shift(cot_prev[:cut], 1), y_shift(cot_next[cut:], -1)], axis=0)
    cot_mine = jnp.concatenate([masked_cot, cot_prev, cot_next, cot_far], axis=0)
    all_cot = jnp.concatenate([cot_mine, core_swap(cot_mine)], axis=0)
    out_part, in_part, gate_term, up_term, down_term = expert_work(
        all_rows, all_cot, gate_w, up_w, down_w
    )
    half = out_part.shape[0] // 2
    outputs = scatter_rows(out_part[half:], out_part[:half])[:slots]
    input_grads = scatter_rows(*in_part)[:slots]
    gate_grad = gate_term.astype(jnp.bfloat16)
    up_grad = up_term.astype(jnp.bfloat16)
    down_grad = down_term.astype(jnp.bfloat16)
    return (outputs[None], input_grads[None], gate_grad[None], up_grad[None], down_grad[None])


def solution(mesh):
    chips = mesh.shape["dp"] // 2
    split = Mesh(mesh.devices.reshape(mesh.shape["expert"], chips, 2), ("expert", "y", "core"))
    rows = P("expert", ("y", "core"), None)
    cols = P("expert", None, ("y", "core"))

    return jax.shard_map(
        shards,
        mesh=split,
        in_specs=(rows, rows, P(), cols, cols, rows),
        out_specs=(rows, rows, cols, cols, rows),
        check_vma=False,
    )
```
